512 devices in a mesh: section: 8 (over x, core), tile: 64 (over z, y).
Axes of the slice: x: 4, y: 8, z: 8, core: 2. Of those that a mesh axis runs over, the one named last changes fastest.
Arguments:
- latents: bfloat16 [8, 2, 512, 384], P(None, None, 'tile'), may hold values from -6 to 6
- col_counts: int32 [64], replicated, may hold values from 1 to 8, 480 in all
- conv_weight: bfloat16 [8, 3, 3, 1152, 384], P('section'), may hold values from -0.0625 to 0.0625
- norm_gain: bfloat16 [8, 384], P('section'), may hold values from 0.099609375 to 1.8984375
Outputs:
- decoded: bfloat16 [8, 2, 512, 384], P('section', None, 'tile')
The draws below stay inside these ranges and needn't reach their ends.
Inputs may be any that keep to these rules, and one draw needn't show every extreme that they name: Strip t holds col_counts[t] image columns; the counts sum to 480 and some strip holds 8.
All inputs are finite; a program needn't handle non-finite values.
Results may differ from the reference program's by a relative error of at most 0.013.
Values may be sent and summed in bfloat16 or wider, within the bound.
No kernel may reach another device: no remote copies, remote signals or barrier semaphores. Data moves between devices by JAX's collectives and lax.ppermute only.
A program may use at most 64 MiB of HBM per device.

```python
import math
import jax
import jax.numpy as jnp
import numpy as np
from jax import lax

CH = 384
ROWS = 2
COLS_DEV = 8
FRAMES = 8
LAYERS = 8
TOTAL_COLS = 480
N_TILE = 64


def shard_levels(key, extent, cuts, smallest, high):
    loudness, own = 1.0, jax.random.fold_in(key, 6)
    for position, blocks in cuts:
        draws = jnp.exp(jax.random.uniform(jax.random.fold_in(own, position), (blocks,), jnp.float32, smallest / len(cuts), high / len(cuts)))
        loudness = loudness * jnp.repeat(draws, extent[position] // blocks).reshape([-1 if axis == position else 1 for axis in range(len(extent))])
    return loudness


def length_profile(amount, total, limit, skew):
    portions = [(1 << 20) // math.isqrt(grade ** skew) + 1 for grade in range(2, amount + 1)]
    rest, given = total - limit - (amount - 1), [1] * (amount - 1)
    while rest > 0:
        candidates = [i for i in range(amount - 1) if given[i] < limit]
        mass, remaining = sum([portions[i] for i in candidates]), rest
        for i in candidates:
            extra = min(limit - given[i], max(1, remaining * portions[i] // mass), rest)
            given[i] = given[i] + extra
            rest = rest - extra
    return np.array([limit] + given)


def uneven(rng, count, total, most, lean):
    if count == 2:
        one = jax.random.randint(rng, (), max(1, total - most), min(most, total - 1) + 1)
        return jnp.stack([one, total - one])
    lengths = jnp.asarray(length_profile(count, total, most, lean), jnp.int32)
    pairs = (count - 1) // 2
    donor, taker = lengths[1:1 + 2 * pairs:2], lengths[2:2 + 2 * pairs:2]
    slack = jnp.minimum(donor - 1, most - taker)
    passed = jax.random.randint(jax.random.fold_in(rng, 1), (pairs,), 0, 1 << 20) % (slack + 1)
    lengths = lengths.at[1:1 + 2 * pairs:2].set(donor - passed).at[2:2 + 2 * pairs:2].set(taker + passed)
    return lengths[jax.random.permutation(jax.random.fold_in(rng, 2), count)]


def centred(stream_key, extent, scale, bound, shards=(), held_as=jnp.bfloat16):
    drawn = scale * jax.random.normal(stream_key, extent, jnp.float32)
    if shards:
        drawn = drawn * shard_levels(stream_key, extent, shards, -0.22, 0.18)
    return jnp.clip(drawn, -bound, bound).astype(held_as)


def setup_inputs(seed: int = 0) -> dict:
    seeds = jax.random.split(jax.random.key(seed), 5)
    return {
        "latents": centred(seeds[0], (FRAMES, ROWS, N_TILE * COLS_DEV, CH), 1.0, 6.0, ((2, 64),)),
        "col_counts": uneven(seeds[1], N_TILE, TOTAL_COLS, COLS_DEV, 1).astype(jnp.int32),
        "conv_weight": centred(seeds[2], (LAYERS, 3, 3, 3 * CH, CH), (27 * CH) ** -0.5, 0.0625, ((0, 8),)),
        "norm_gain": jnp.clip(1.0 + 0.18 * jax.random.normal(seeds[3], (LAYERS, CH), jnp.float32), 0.099609375, 1.8984375).astype(jnp.bfloat16),
    }


def norm_silu(values, gain):
    widened = values.astype(jnp.float32)
    scaled = widened * lax.rsqrt(lax.optimization_barrier(jnp.mean(widened * widened, axis=-1, keepdims=True)) + 1e-06) * gain.astype(jnp.float32)
    return jax.nn.silu(scaled).astype(jnp.bfloat16)

def causal_conv(activated, kernel):
    frame_count, row_count, col_count, channels = activated.shape
    padded = jnp.pad(activated, ((2, 0), (1, 1), (1, 1), (0, 0)))
    joined = jnp.concatenate([padded[:, :, 0:col_count], padded[:, :, 1:col_count + 1], padded[:, :, 2:col_count + 2]], axis=-1)
    summed = jnp.zeros((frame_count, row_count, col_count, kernel.shape[-1]), jnp.float32)
    for frame_tap in range(3):
        for row_tap in range(3):
            summed = summed + jnp.dot(joined[frame_tap:frame_tap + frame_count, row_tap:row_tap + row_count], kernel[frame_tap, row_tap], preferred_element_type=jnp.float32)
    return summed

def reference(latents, col_counts, conv_weight, norm_gain):
    col_owner = jnp.repeat(jnp.arange(N_TILE, dtype=jnp.int32), col_counts, total_repeat_length=TOTAL_COLS).astype(jnp.int32)
    owner_starts = (jnp.cumsum(col_counts) - col_counts).astype(jnp.int32)
    local_cols = jnp.arange(TOTAL_COLS, dtype=jnp.int32) - owner_starts[col_owner]
    col_source = (col_owner * COLS_DEV + local_cols).astype(jnp.int32)
    stream_now = jnp.take(latents, col_source, axis=2)
    for block_index in range(LAYERS // 2):
        first_layer = 2 * block_index
        branch = causal_conv(norm_silu(stream_now, norm_gain[first_layer]), conv_weight[first_layer]).astype(jnp.bfloat16)
        second = causal_conv(norm_silu(branch, norm_gain[first_layer + 1]), conv_weight[first_layer + 1])
        stream_now = (stream_now.astype(jnp.float32) + second).astype(jnp.bfloat16)
    placed = jnp.zeros(latents.shape, jnp.bfloat16).at[:, :, col_source].set(stream_now)
    return placed
```

```python
import jax
import jax.numpy as jnp
from jax import lax
from jax.sharding import PartitionSpec as P


def hop(block, pairs, axes):
    return lax.ppermute(block, axes, pairs)


def activate(values, gain):
    widened = values.astype(jnp.float32)
    scaled = widened * lax.rsqrt(jnp.mean(widened * widened, axis=-1, keepdims=True) + 1e-06) * gain
    return jax.nn.silu(scaled).astype(jnp.bfloat16)


def convolve(activated, kernel):
    frames, rows, cols_ext, channels = activated.shape
    cols = cols_ext - 2
    padded = jnp.pad(activated, ((2, 0), (1, 1), (0, 0), (0, 0)))
    taps = []
    for frame_tap in range(3):
        for row_tap in range(3):
            for col_tap in range(3):
                taps.append(
                    padded[frame_tap : frame_tap + frames, row_tap : row_tap + rows, col_tap : col_tap + cols]
                )
    joined = jnp.concatenate(taps, axis=-1).reshape(frames * rows * cols, 27 * channels)
    flat = kernel.reshape(27 * channels, kernel.shape[-1])
    out = jnp.dot(joined, flat, preferred_element_type=jnp.float32)
    return out.reshape(frames, rows, cols, kernel.shape[-1])


def local(latents, col_counts, conv_weight, norm_gain):
    segments = lax.axis_size("section")
    tiles = lax.axis_size("tile")
    segment_index = lax.axis_index("section")
    tile_index = lax.axis_index("tile")
    frames_all, row_count, col_count, channels = latents.shape
    live_cols = col_counts[tile_index]
    kernel = conv_weight[0]
    gain = norm_gain[0].astype(jnp.float32)
    col_live = jnp.arange(col_count)[None, None, :, None] < live_cols
    ext_index = jnp.arange(col_count + 2)[None, None, :, None]
    zero = jnp.zeros((), jnp.bfloat16)
    both = ("section", "tile")

    def edges(block):
        first = block[:, :, 0:1]
        last = lax.dynamic_slice_in_dim(block, live_cols - 1, 1, 2)
        return first, last

    def extend(block, left, right):
        wide = jnp.concatenate([left, block, jnp.zeros_like(left)], axis=2)
        return jnp.where(ext_index == live_cols + 1, right, wide)

    def diagonal(first, last, stage):
        src, dst = stage * tiles, (stage + 1) * tiles
        left = hop(last, [(src + t - 1, dst + t) for t in range(1, tiles)], both)
        right = hop(first, [(src + t + 1, dst + t) for t in range(tiles - 1)], both)
        return left, right

    stream = jnp.where(col_live, latents, zero)
    first, last = edges(stream)
    left = hop(last, [(t - 1, t) for t in range(1, tiles)], "tile")
    right = hop(first, [(t + 1, t) for t in range(tiles - 1)], "tile")
    current = stream
    residual = stream
    for stage in range(segments):
        activated = activate(extend(current, left, right), gain)
        conv_out = convolve(activated, kernel)
        if stage % 2 == 0:
            produced = jnp.where(col_live, conv_out, 0.0).astype(jnp.bfloat16)
        else:
            produced = jnp.where(
                col_live, (residual.astype(jnp.float32) + conv_out).astype(jnp.bfloat16), zero
            )
        if stage == segments - 1:
            break
        first, last = edges(produced)
        left, right = diagonal(first, last, stage)
        nxt = hop(produced, [(stage, stage + 1)], "section")
        if stage % 2 == 1 and stage + 2 < segments:
            residual = hop(produced, [(stage, stage + 2)], "section")
        current = nxt
    final = produced
    result = final[segments - 1 : segments]
    for target in range(segments - 1):
        piece = hop(final[target : target + 1], [(segments - 1, target)], "section")
        result = jnp.where(segment_index == target, piece, result)
    return result


def solution(mesh):
    return jax.shard_map(
        local,
        mesh=mesh,
        in_specs=(
            P(None, None, "tile", None),
            P(),
            P("section", None, None, None, None),
            P("section", None),
        ),
        out_specs=P("section", None, "tile", None),
        check_vma=False,
    )
```

```python
import jax
import jax.numpy as jnp
from jax import lax
from jax.sharding import PartitionSpec as P


def hop(block, pairs, axes):
    return lax.ppermute(block, axes, pairs)


def activate(values, gain):
    widened = values.astype(jnp.float32)
    scaled = widened * lax.rsqrt(jnp.mean(widened * widened, axis=-1, keepdims=True) + 1e-06) * gain
    return jax.nn.silu(scaled).astype(jnp.bfloat16)


def convolve(activated, kernel):
    padded = jnp.pad(activated, ((2, 0), (1, 1), (0, 0), (0, 0)))
    taps = kernel.reshape(3, 3, 3, activated.shape[-1], kernel.shape[-1])
    out = lax.conv_general_dilated(
        padded[None],
        taps,
        window_strides=(1, 1, 1),
        padding="VALID",
        dimension_numbers=("NDHWC", "DHWIO", "NDHWC"),
        preferred_element_type=jnp.float32,
    )
    return out[0]


def local(latents, col_counts, conv_weight, norm_gain):
    segments = lax.axis_size("section")
    tiles = lax.axis_size("tile")
    segment_index = lax.axis_index("section")
    tile_index = lax.axis_index("tile")
    frames_all, row_count, col_count, channels = latents.shape
    live_cols = col_counts[tile_index]
    kernel = conv_weight[0]
    gain = norm_gain[0].astype(jnp.float32)
    col_live = jnp.arange(col_count)[None, None, :, None] < live_cols
    ext_index = jnp.arange(col_count + 2)[None, None, :, None]
    zero = jnp.zeros((), jnp.bfloat16)
    both = ("section", "tile")

    def edges(block):
        first = block[:, :, 0:1]
        last = lax.dynamic_slice_in_dim(block, live_cols - 1, 1, 2)
        return first, last

    def extend(block, left, right):
        wide = jnp.concatenate([left, block, jnp.zeros_like(left)], axis=2)
        return jnp.where(ext_index == live_cols + 1, right, wide)

    def diagonal(first, last, stage):
        src, dst = stage * tiles, (stage + 1) * tiles
        left = hop(last, [(src + t - 1, dst + t) for t in range(1, tiles)], both)
        right = hop(first, [(src + t + 1, dst + t) for t in range(tiles - 1)], both)
        return left, right

    stream = jnp.where(col_live, latents, zero)
    first, last = edges(stream)
    left = hop(last, [(t - 1, t) for t in range(1, tiles)], "tile")
    right = hop(first, [(t + 1, t) for t in range(tiles - 1)], "tile")
    current = stream
    residual = stream
    for stage in range(segments):
        activated = activate(extend(current, left, right), gain)
        conv_out = convolve(activated, kernel)
        if stage % 2 == 0:
            produced = jnp.where(col_live, conv_out, 0.0).astype(jnp.bfloat16)
        else:
            produced = jnp.where(
                col_live, (residual.astype(jnp.float32) + conv_out).astype(jnp.bfloat16), zero
            )
        if stage == segments - 1:
            break
        first, last = edges(produced)
        left, right = diagonal(first, last, stage)
        nxt = hop(produced, [(stage, stage + 1)], "section")
        if stage % 2 == 1 and stage + 2 < segments:
            residual = hop(produced, [(stage, stage + 2)], "section")
        current = nxt
    final = produced
    spread = lax.all_to_all(final, "section", 0, 0, tiled=True)
    return spread[segments - 1 : segments]

def solution(mesh):
    return jax.shard_map(
        local,
        mesh=mesh,
        in_specs=(
            P(None, None, "tile", None),
            P(),
            P("section", None, None, None, None),
            P("section", None),
        ),
        out_specs=P("section", None, "tile", None),
        check_vma=False,
    )
```

```python
import jax
import jax.numpy as jnp
from jax import lax
from jax.sharding import PartitionSpec as P


def hop(block, pairs, axes):
    return lax.ppermute(block, axes, pairs)


def activate(values, gain):
    widened = values.astype(jnp.float32)
    scaled = widened * lax.rsqrt(jnp.mean(widened * widened, axis=-1, keepdims=True) + 1e-06) * gain
    return jax.nn.silu(scaled).astype(jnp.bfloat16)


def convolve(activated, kernel):
    frames, rows, cols_ext, channels = activated.shape
    cols = cols_ext - 2
    padded = jnp.pad(activated, ((2, 0), (1, 1), (0, 0), (0, 0)))
    taps = []
    for frame_tap in range(3):
        for row_tap in range(3):
            for col_tap in range(3):
                taps.append(
                    padded[frame_tap : frame_tap + frames, row_tap : row_tap + rows, col_tap : col_tap + cols]
                )
    joined = jnp.concatenate(taps, axis=-1).reshape(frames * rows * cols, 27 * channels)
    flat = kernel.reshape(27 * channels, kernel.shape[-1])
    out = jnp.dot(joined, flat, preferred_element_type=jnp.float32)
    return out.reshape(frames, rows, cols, kernel.shape[-1])


def local(latents, col_counts, conv_weight, norm_gain):
    segments = lax.axis_size("section")
    tiles = lax.axis_size("tile")
    segment_index = lax.axis_index("section")
    tile_index = lax.axis_index("tile")
    frames_all, row_count, col_count, channels = latents.shape
    live_cols = col_counts[tile_index]
    kernel = conv_weight[0]
    gain = norm_gain[0].astype(jnp.float32)
    col_live = jnp.arange(col_count)[None, None, :, None] < live_cols
    ext_index = jnp.arange(col_count + 2)[None, None, :, None]
    zero = jnp.zeros((), jnp.bfloat16)
    both = ("section", "tile")

    def edges(block):
        first = block[:, :, 0:1]
        last = lax.dynamic_slice_in_dim(block, live_cols - 1, 1, 2)
        return first, last

    def extend(block, left, right):
        wide = jnp.concatenate([left, block, jnp.zeros_like(left)], axis=2)
        return jnp.where(ext_index == live_cols + 1, right, wide)

    def diagonal(first, last, stage):
        src, dst = stage * tiles, (stage + 1) * tiles
        left = hop(last, [(src + t - 1, dst + t) for t in range(1, tiles)], both)
        right = hop(first, [(src + t + 1, dst + t) for t in range(tiles - 1)], both)
        return left, right

    stream = jnp.where(col_live, latents, zero)
    first, last = edges(stream)
    left = hop(last, [(t - 1, t) for t in range(1, tiles)], "tile")
    right = hop(first, [(t + 1, t) for t in range(tiles - 1)], "tile")
    current = stream
    residual = stream
    for stage in range(segments):
        activated = activate(extend(current, left, right), gain)
        conv_out = convolve(activated, kernel)
        if stage % 2 == 0:
            produced = jnp.where(col_live, conv_out, 0.0).astype(jnp.bfloat16)
        else:
            produced = jnp.where(
                col_live, (residual.astype(jnp.float32) + conv_out).astype(jnp.bfloat16), zero
            )
        if stage == segments - 1:
            break
        first, last = edges(produced)
        left, right = diagonal(first, last, stage)
        nxt = hop(produced, [(stage, stage + 1)], "section")
        if stage % 2 == 1 and stage + 2 < segments:
            residual = hop(produced, [(stage, stage + 2)], "section")
        current = nxt
    final = produced
    spread = lax.all_to_all(final, "section", 0, 0, tiled=True)
    return spread[segments - 1 : segments]

def solution(mesh):
    return jax.shard_map(
        local,
        mesh=mesh,
        in_specs=(
            P(None, None, "tile", None),
            P(),
            P("section", None, None, None, None),
            P("section", None),
        ),
        out_specs=P("section", None, "tile", None),
        check_vma=False,
    )
```

```python
import jax
import jax.numpy as jnp
from jax import lax
from jax.sharding import PartitionSpec as P


def hop(block, pairs, axes):
    return lax.ppermute(block, axes, pairs)


def activate(values, gain):
    widened = values.astype(jnp.float32)
    scaled = widened * lax.rsqrt(jnp.mean(widened * widened, axis=-1, keepdims=True) + 1e-06) * gain
    return jax.nn.silu(scaled).astype(jnp.bfloat16)


def convolve(activated, kernel):
    frames, rows, cols_ext, channels = activated.shape
    cols = cols_ext - 2
    padded = jnp.pad(activated, ((2, 0), (1, 1), (0, 0), (0, 0)))
    taps = []
    for frame_tap in range(3):
        for row_tap in range(3):
            for col_tap in range(3):
                taps.append(
                    padded[frame_tap : frame_tap + frames, row_tap : row_tap + rows, col_tap : col_tap + cols]
                )
    joined = jnp.concatenate(taps, axis=-1).reshape(frames * rows * cols, 27 * channels)
    flat = kernel.reshape(27 * channels, kernel.shape[-1])
    out = jnp.dot(joined, flat, preferred_element_type=jnp.float32)
    return out.reshape(frames, rows, cols, kernel.shape[-1])


def edge_terms(left, right, kernel, channels):
    def taps(column):
        frames, rows = column.shape[0], column.shape[1]
        padded = jnp.pad(column[:, :, 0], ((2, 0), (1, 1), (0, 0)))
        pieces = [
            padded[frame_tap : frame_tap + frames, row_tap : row_tap + rows]
            for frame_tap in range(3)
            for row_tap in range(3)
        ]
        return jnp.concatenate(pieces, axis=-1).reshape(frames * rows, 9 * channels)

    lhs_left, lhs_right = taps(left), taps(right)
    zeros = jnp.zeros_like(lhs_left)
    lhs = jnp.concatenate(
        [jnp.concatenate([lhs_left, zeros], axis=1), jnp.concatenate([zeros, lhs_right], axis=1)], axis=0
    )
    weights = jnp.concatenate(
        [
            kernel[:, :, 0:channels].reshape(9 * channels, kernel.shape[-1]),
            kernel[:, :, 2 * channels : 3 * channels].reshape(9 * channels, kernel.shape[-1]),
        ],
        axis=0,
    )
    out = jnp.dot(lhs, weights, preferred_element_type=jnp.float32)
    frames, rows = left.shape[0], left.shape[1]
    return out[: frames * rows].reshape(frames, rows, 1, -1), out[frames * rows :].reshape(frames, rows, 1, -1)


def local(latents, col_counts, conv_weight, norm_gain):
    segments = lax.axis_size("section")
    tiles = lax.axis_size("tile")
    segment_index = lax.axis_index("section")
    tile_index = lax.axis_index("tile")
    frames_all, row_count, col_count, channels = latents.shape
    live_cols = col_counts[tile_index]
    kernel = conv_weight[0]
    gain = norm_gain[0].astype(jnp.float32)
    col_live = jnp.arange(col_count)[None, None, :, None] < live_cols
    slot_index = jnp.arange(col_count)[None, None, :, None]
    zero = jnp.zeros((), jnp.bfloat16)
    both = ("section", "tile")

    def edges(block):
        first = block[:, :, 0:1]
        last = lax.dynamic_slice_in_dim(block, live_cols - 1, 1, 2)
        return first, last

    def diagonal(first, last, stage):
        src, dst = stage * tiles, (stage + 1) * tiles
        left = hop(last, [(src + t - 1, dst + t) for t in range(1, tiles)], both)
        right = hop(first, [(src + t + 1, dst + t) for t in range(tiles - 1)], both)
        return left, right

    stream = jnp.where(col_live, latents, zero)
    first, last = edges(stream)
    left = hop(last, [(t - 1, t) for t in range(1, tiles)], "tile")
    right = hop(first, [(t + 1, t) for t in range(tiles - 1)], "tile")
    current = stream
    residual = stream
    for stage in range(segments):
        activated = jnp.pad(activate(current, gain), ((0, 0), (0, 0), (1, 1), (0, 0)))
        conv_out = convolve(activated, kernel)
        conv_out, left, right = lax.optimization_barrier((conv_out, left, right))
        term_left, term_right = edge_terms(activate(left, gain), activate(right, gain), kernel, channels)
        conv_out = (
            conv_out
            + jnp.where(slot_index == 0, term_left, 0.0)
            + jnp.where(slot_index == live_cols - 1, term_right, 0.0)
        )
        if stage % 2 == 0:
            produced = jnp.where(col_live, conv_out, 0.0).astype(jnp.bfloat16)
        else:
            produced = jnp.where(
                col_live, (residual.astype(jnp.float32) + conv_out).astype(jnp.bfloat16), zero
            )
        if stage == segments - 1:
            break
        first, last = edges(produced)
        if stage % 2 == 0:
            both_next = hop(jnp.stack([produced, residual]), [(stage, stage + 1)], "section")
            left, right = diagonal(first, last, stage)
            current, residual = both_next[0], both_next[1]
        else:
            current = hop(produced, [(stage, stage + 1)], "section")
            left, right = diagonal(first, last, stage)
            residual = current
    final = produced
    spread = lax.all_to_all(final, "section", 0, 0, tiled=True)
    return spread[segments - 1 : segments]

def solution(mesh):
    return jax.shard_map(
        local,
        mesh=mesh,
        in_specs=(
            P(None, None, "tile", None),
            P(),
            P("section", None, None, None, None),
            P("section", None),
        ),
        out_specs=P("section", None, "tile", None),
        check_vma=False,
    )
```

```python
import jax
import jax.numpy as jnp
from jax import lax
from jax.sharding import PartitionSpec as P


def hop(block, pairs, axes):
    return lax.ppermute(block, axes, pairs)


def activate(values, gain):
    widened = values.astype(jnp.float32)
    scaled = widened * lax.rsqrt(jnp.mean(widened * widened, axis=-1, keepdims=True) + 1e-06) * gain
    return jax.nn.silu(scaled).astype(jnp.bfloat16)


def convolve(activated, kernel):
    frames, rows, cols_ext, channels = activated.shape
    cols = cols_ext - 2
    padded = jnp.pad(activated, ((2, 0), (1, 1), (0, 0), (0, 0)))
    taps = []
    for frame_tap in range(3):
        for row_tap in range(3):
            for col_tap in range(3):
                taps.append(
                    padded[frame_tap : frame_tap + frames, row_tap : row_tap + rows, col_tap : col_tap + cols]
                )
    joined = jnp.concatenate(taps, axis=-1).reshape(frames * rows * cols, 27 * channels)
    flat = kernel.reshape(27 * channels, kernel.shape[-1])
    out = jnp.dot(joined, flat, preferred_element_type=jnp.float32)
    return out.reshape(frames, rows, cols, kernel.shape[-1])


def edge_terms(left, right, kernel):
    gap = jnp.zeros_like(left)
    out = convolve(jnp.concatenate([left, gap, gap, right], axis=2), kernel)
    return out[:, :, 0:1], out[:, :, 1:2]


def local(latents, col_counts, conv_weight, norm_gain):
    segments = lax.axis_size("section")
    tiles = lax.axis_size("tile")
    segment_index = lax.axis_index("section")
    tile_index = lax.axis_index("tile")
    frames_all, row_count, col_count, channels = latents.shape
    live_cols = col_counts[tile_index]
    kernel = conv_weight[0]
    gain = norm_gain[0].astype(jnp.float32)
    col_live = jnp.arange(col_count)[None, None, :, None] < live_cols
    slot_index = jnp.arange(col_count)[None, None, :, None]
    zero = jnp.zeros((), jnp.bfloat16)
    both = ("section", "tile")

    def edges(block):
        first = block[:, :, 0:1]
        last = lax.dynamic_slice_in_dim(block, live_cols - 1, 1, 2)
        return first, last

    def diagonal(first, last, stage):
        src, dst = stage * tiles, (stage + 1) * tiles
        left = hop(last, [(src + t - 1, dst + t) for t in range(1, tiles)], both)
        right = hop(first, [(src + t + 1, dst + t) for t in range(tiles - 1)], both)
        return left, right

    stream = jnp.where(col_live, latents, zero)
    first, last = edges(stream)
    left = hop(last, [(t - 1, t) for t in range(1, tiles)], "tile")
    right = hop(first, [(t + 1, t) for t in range(tiles - 1)], "tile")
    current = stream
    residual = stream
    for stage in range(segments):
        activated = jnp.pad(activate(current, gain), ((0, 0), (0, 0), (1, 1), (0, 0)))
        conv_out = convolve(activated, kernel)
        conv_out, left, right = lax.optimization_barrier((conv_out, left, right))
        term_left, term_right = edge_terms(activate(left, gain), activate(right, gain), kernel)
        conv_out = (
            conv_out
            + jnp.where(slot_index == 0, term_left, 0.0)
            + jnp.where(slot_index == live_cols - 1, term_right, 0.0)
        )
        if stage % 2 == 0:
            produced = jnp.where(col_live, conv_out, 0.0).astype(jnp.bfloat16)
        else:
            produced = jnp.where(
                col_live, (residual.astype(jnp.float32) + conv_out).astype(jnp.bfloat16), zero
            )
        if stage == segments - 1:
            break
        first, last = edges(produced)
        if stage % 2 == 0:
            both_next = hop(jnp.stack([produced, residual]), [(stage, stage + 1)], "section")
            left, right = diagonal(first, last, stage)
            current, residual = both_next[0], both_next[1]
        else:
            current = hop(produced, [(stage, stage + 1)], "section")
            left, right = diagonal(first, last, stage)
            residual = current
    final = produced
    spread = lax.all_to_all(final, "section", 0, 0, tiled=True)
    return spread[segments - 1 : segments]

def solution(mesh):
    return jax.shard_map(
        local,
        mesh=mesh,
        in_specs=(
            P(None, None, "tile", None),
            P(),
            P("section", None, None, None, None),
            P("section", None),
        ),
        out_specs=P("section", None, "tile", None),
        check_vma=False,
    )
```

```python
import jax
import jax.numpy as jnp
from jax import lax
from jax.sharding import PartitionSpec as P


def hop(block, pairs, axes):
    return lax.ppermute(block, axes, pairs)


def activate(values, gain):
    widened = values.astype(jnp.float32)
    scaled = widened * lax.rsqrt(jnp.mean(widened * widened, axis=-1, keepdims=True) + 1e-06) * gain
    return jax.nn.silu(scaled).astype(jnp.bfloat16)


def convolve(activated, kernel):
    frames, rows, cols_ext, channels = activated.shape
    cols = cols_ext - 2
    padded = jnp.pad(activated, ((2, 0), (1, 1), (0, 0), (0, 0)))
    taps = []
    for frame_tap in range(3):
        for row_tap in range(3):
            for col_tap in range(3):
                taps.append(
                    padded[frame_tap : frame_tap + frames, row_tap : row_tap + rows, col_tap : col_tap + cols]
                )
    joined = jnp.concatenate(taps, axis=-1).reshape(frames * rows * cols, 27 * channels)
    flat = kernel.reshape(27 * channels, kernel.shape[-1])
    out = jnp.dot(joined, flat, preferred_element_type=jnp.float32)
    return out.reshape(frames, rows, cols, kernel.shape[-1])


def local(latents, col_counts, conv_weight, norm_gain):
    segments = lax.axis_size("section")
    tiles = lax.axis_size("tile")
    segment_index = lax.axis_index("section")
    tile_index = lax.axis_index("tile")
    frames_all, row_count, col_count, channels = latents.shape
    live_cols = col_counts[tile_index]
    kernel = conv_weight[0]
    gain = norm_gain[0].astype(jnp.float32)
    col_live = jnp.arange(col_count)[None, None, :, None] < live_cols
    ext_index = jnp.arange(col_count + 2)[None, None, :, None]
    zero = jnp.zeros((), jnp.bfloat16)
    both = ("section", "tile")

    def edges(block):
        first = block[:, :, 0:1]
        last = lax.dynamic_slice_in_dim(block, live_cols - 1, 1, 2)
        return first, last

    def extend(block, left, right):
        wide = jnp.concatenate([left, block, jnp.zeros_like(left)], axis=2)
        return jnp.where(ext_index == live_cols + 1, right, wide)

    def diagonal(first, last, stage):
        src, dst = stage * tiles, (stage + 1) * tiles
        left = hop(last, [(src + t - 1, dst + t) for t in range(1, tiles)], both)
        right = hop(first, [(src + t + 1, dst + t) for t in range(tiles - 1)], both)
        return left, right

    from_left = hop(latents, [(t - 1, t) for t in range(1, tiles)], "tile")
    from_right = hop(latents[:, :, 0:1], [(t + 1, t) for t in range(tiles - 1)], "tile")
    left_count = col_counts[jnp.maximum(tile_index - 1, 0)]
    left = lax.dynamic_slice_in_dim(from_left, left_count - 1, 1, 2)
    right = from_right
    stream = jnp.where(col_live, latents, zero)
    current = stream
    residual = stream
    for stage in range(segments):
        activated = activate(extend(current, left, right), gain)
        conv_out = convolve(activated, kernel)
        if stage % 2 == 0:
            produced = jnp.where(col_live, conv_out, 0.0).astype(jnp.bfloat16)
        else:
            produced = jnp.where(
                col_live, (residual.astype(jnp.float32) + conv_out).astype(jnp.bfloat16), zero
            )
        if stage == segments - 1:
            break
        first, last = edges(produced)
        left, right = diagonal(first, last, stage)
        nxt = hop(produced, [(stage, stage + 1)], "section")
        if stage % 2 == 1 and stage + 2 < segments:
            residual = hop(produced, [(stage, stage + 2)], "section")
        current = nxt
    final = produced
    spread = lax.all_to_all(final, "section", 0, 0, tiled=True)
    return spread[segments - 1 : segments]

def solution(mesh):
    return jax.shard_map(
        local,
        mesh=mesh,
        in_specs=(
            P(None, None, "tile", None),
            P(),
            P("section", None, None, None, None),
            P("section", None),
        ),
        out_specs=P("section", None, "tile", None),
        check_vma=False,
    )
```

```python
import jax
import jax.numpy as jnp
from jax import lax
from jax.sharding import PartitionSpec as P


def hop(block, pairs, axes):
    return lax.ppermute(block, axes, pairs)


def activate(values, gain):
    widened = values.astype(jnp.float32)
    scaled = widened * lax.rsqrt(jnp.mean(widened * widened, axis=-1, keepdims=True) + 1e-06) * gain
    return jax.nn.silu(scaled).astype(jnp.bfloat16)


def convolve(activated, kernel):
    frames, rows, cols_ext, channels = activated.shape
    cols = cols_ext - 2
    padded = jnp.pad(activated, ((2, 0), (1, 1), (0, 0), (0, 0)))
    shifted = jnp.concatenate([padded[:, :, k : k + cols] for k in range(3)], axis=-1)
    shifted = lax.optimization_barrier(shifted)
    taps = [
        shifted[frame_tap : frame_tap + frames, row_tap : row_tap + rows]
        for frame_tap in range(3)
        for row_tap in range(3)
    ]
    joined = jnp.concatenate(taps, axis=-1).reshape(frames * rows * cols, 27 * channels)
    flat = kernel.reshape(27 * channels, kernel.shape[-1])
    out = jnp.dot(joined, flat, preferred_element_type=jnp.float32)
    return out.reshape(frames, rows, cols, kernel.shape[-1])


def local(latents, col_counts, conv_weight, norm_gain):
    segments = lax.axis_size("section")
    tiles = lax.axis_size("tile")
    segment_index = lax.axis_index("section")
    tile_index = lax.axis_index("tile")
    frames_all, row_count, col_count, channels = latents.shape
    live_cols = col_counts[tile_index]
    kernel = conv_weight[0]
    gain = norm_gain[0].astype(jnp.float32)
    col_live = jnp.arange(col_count)[None, None, :, None] < live_cols
    ext_index = jnp.arange(col_count + 2)[None, None, :, None]
    zero = jnp.zeros((), jnp.bfloat16)
    both = ("section", "tile")

    def edges(block):
        first = block[:, :, 0:1]
        last = lax.dynamic_slice_in_dim(block, live_cols - 1, 1, 2)
        return first, last

    def extend(block, left, right):
        wide = jnp.concatenate([left, block, jnp.zeros_like(left)], axis=2)
        return jnp.where(ext_index == live_cols + 1, right, wide)

    def diagonal(first, last, stage):
        src, dst = stage * tiles, (stage + 1) * tiles
        left = hop(last, [(src + t - 1, dst + t) for t in range(1, tiles)], both)
        right = hop(first, [(src + t + 1, dst + t) for t in range(tiles - 1)], both)
        return left, right

    from_left = hop(latents, [(t - 1, t) for t in range(1, tiles)], "tile")
    from_right = hop(latents[:, :, 0:1], [(t + 1, t) for t in range(tiles - 1)], "tile")
    left_count = col_counts[jnp.maximum(tile_index - 1, 0)]
    left = lax.dynamic_slice_in_dim(from_left, left_count - 1, 1, 2)
    right = from_right
    stream = jnp.where(col_live, latents, zero)
    current = stream
    residual = stream
    for stage in range(segments):
        activated = activate(extend(current, left, right), gain)
        conv_out = convolve(activated, kernel)
        if stage % 2 == 0:
            produced = jnp.where(col_live, conv_out, 0.0).astype(jnp.bfloat16)
        else:
            produced = jnp.where(
                col_live, (residual.astype(jnp.float32) + conv_out).astype(jnp.bfloat16), zero
            )
        if stage == segments - 1:
            break
        first, last = edges(produced)
        left, right = diagonal(first, last, stage)
        nxt = hop(produced, [(stage, stage + 1)], "section")
        if stage % 2 == 1 and stage + 2 < segments:
            residual = hop(produced, [(stage, stage + 2)], "section")
        current = nxt
    final = produced
    spread = lax.all_to_all(final, "section", 0, 0, tiled=True)
    return spread[segments - 1 : segments]

def solution(mesh):
    return jax.shard_map(
        local,
        mesh=mesh,
        in_specs=(
            P(None, None, "tile", None),
            P(),
            P("section", None, None, None, None),
            P("section", None),
        ),
        out_specs=P("section", None, "tile", None),
        check_vma=False,
    )
```

```python
import jax
import jax.numpy as jnp
from jax import lax
from jax.sharding import PartitionSpec as P


def hop(block, pairs, axes):
    return lax.ppermute(block, axes, pairs)


def activate(values, gain):
    widened = values.astype(jnp.float32)
    scaled = widened * lax.rsqrt(jnp.mean(widened * widened, axis=-1, keepdims=True) + 1e-06) * gain
    return jax.nn.silu(scaled).astype(jnp.bfloat16)


def convolve(activated, kernel):
    frames, rows, cols_ext, channels = activated.shape
    cols = cols_ext - 2
    padded = jnp.pad(activated, ((2, 0), (1, 1), (0, 0), (0, 0)))
    shifted = jnp.concatenate([padded[:, :, k : k + cols] for k in range(3)], axis=-1)
    shifted = lax.optimization_barrier(shifted)
    taps = [
        shifted[frame_tap : frame_tap + frames, row_tap : row_tap + rows]
        for frame_tap in range(3)
        for row_tap in range(3)
    ]
    joined = jnp.concatenate(taps, axis=-1).reshape(frames * rows * cols, 27 * channels)
    flat = kernel.reshape(27 * channels, kernel.shape[-1])
    out = jnp.dot(joined, flat, preferred_element_type=jnp.float32)
    return out.reshape(frames, rows, cols, kernel.shape[-1])


def local(latents, col_counts, conv_weight, norm_gain):
    segments = lax.axis_size("section")
    tiles = lax.axis_size("tile")
    segment_index = lax.axis_index("section")
    tile_index = lax.axis_index("tile")
    frames_all, row_count, col_count, channels = latents.shape
    live_cols = col_counts[tile_index]
    kernel = conv_weight[0]
    gain = norm_gain[0].astype(jnp.float32)
    col_live = jnp.arange(col_count)[None, None, :, None] < live_cols
    ext_index = jnp.arange(col_count + 2)[None, None, :, None]
    zero = jnp.zeros((), jnp.bfloat16)
    both = ("section", "tile")

    def edges(block):
        first = block[:, :, 0:1]
        last = lax.dynamic_slice_in_dim(block, live_cols - 1, 1, 2)
        return first, last

    def extend(block, left, right):
        wide = jnp.concatenate([left, block, jnp.zeros_like(left)], axis=2)
        return jnp.where(ext_index == live_cols + 1, right, wide)

    def diagonal(first, last, stage):
        src, dst = stage * tiles, (stage + 1) * tiles
        left = hop(last, [(src + t - 1, dst + t) for t in range(1, tiles)], both)
        right = hop(first, [(src + t + 1, dst + t) for t in range(tiles - 1)], both)
        return left, right

    from_left = hop(latents, [(t - 1, t) for t in range(1, tiles)], "tile")
    from_right = hop(latents[:, :, 0:1], [(t + 1, t) for t in range(tiles - 1)], "tile")
    left_count = col_counts[jnp.maximum(tile_index - 1, 0)]
    left = lax.dynamic_slice_in_dim(from_left, left_count - 1, 1, 2)
    right = from_right
    stream = jnp.where(col_live, latents, zero)
    current = stream
    residual = stream
    for stage in range(segments):
        strip = lax.optimization_barrier(activate(current, gain))
        activated = extend(strip, activate(left, gain), activate(right, gain))
        conv_out = convolve(activated, kernel)
        if stage % 2 == 0:
            produced = jnp.where(col_live, conv_out, 0.0).astype(jnp.bfloat16)
        else:
            produced = jnp.where(
                col_live, (residual.astype(jnp.float32) + conv_out).astype(jnp.bfloat16), zero
            )
        if stage == segments - 1:
            break
        first, last = edges(produced)
        left, right = diagonal(first, last, stage)
        nxt = hop(produced, [(stage, stage + 1)], "section")
        if stage % 2 == 1 and stage + 2 < segments:
            residual = hop(produced, [(stage, stage + 2)], "section")
        current = nxt
    final = produced
    spread = lax.all_to_all(final, "section", 0, 0, tiled=True)
    return spread[segments - 1 : segments]

def solution(mesh):
    return jax.shard_map(
        local,
        mesh=mesh,
        in_specs=(
            P(None, None, "tile", None),
            P(),
            P("section", None, None, None, None),
            P("section", None),
        ),
        out_specs=P("section", None, "tile", None),
        check_vma=False,
    )
```

```python
import jax
import jax.numpy as jnp
from jax import lax
from jax.sharding import PartitionSpec as P


def hop(block, pairs, axes):
    return lax.ppermute(block, axes, pairs)


def activate(values, gain):
    widened = values.astype(jnp.float32)
    scaled = widened * lax.rsqrt(jnp.mean(widened * widened, axis=-1, keepdims=True) + 1e-06) * gain
    return jax.nn.silu(scaled).astype(jnp.bfloat16)


def convolve(activated, kernel):
    frames, rows, cols_ext, channels = activated.shape
    cols = cols_ext - 2
    padded = jnp.pad(activated, ((2, 0), (1, 1), (0, 0), (0, 0)))
    shifted = jnp.concatenate([padded[:, :, k : k + cols] for k in range(3)], axis=-1)
    shifted = lax.optimization_barrier(shifted)
    taps = [
        shifted[frame_tap : frame_tap + frames, row_tap : row_tap + rows]
        for frame_tap in range(3)
        for row_tap in range(3)
    ]
    joined = jnp.concatenate(taps, axis=-1).reshape(frames * rows * cols, 27 * channels)
    flat = kernel.reshape(27 * channels, kernel.shape[-1])
    out = jnp.dot(joined, flat, preferred_element_type=jnp.float32)
    return out.reshape(frames, rows, cols, kernel.shape[-1])


GHOST = 4


def local(latents, col_counts, conv_weight, norm_gain):
    segments = lax.axis_size("section")
    tiles = lax.axis_size("tile")
    tile_index = lax.axis_index("tile")
    frames_all, row_count, col_count, channels = latents.shape
    live_cols = col_counts[tile_index]
    kernel = conv_weight[0]
    gain = norm_gain[0].astype(jnp.float32)
    zero = jnp.zeros((), jnp.bfloat16)
    both = ("section", "tile")
    first_tile = tile_index == 0
    last_tile = tile_index == tiles - 1

    from_left = hop(latents, [(t - 1, t) for t in range(1, tiles)], "tile")
    from_right = hop(latents, [(t + 1, t) for t in range(tiles - 1)], "tile")
    left_count = col_counts[jnp.maximum(tile_index - 1, 0)]
    strip = jnp.where(jnp.arange(col_count)[None, None, :, None] < live_cols, latents, zero)

    def assemble(strip, left, right, depth):
        wide = jnp.concatenate([left, strip, jnp.zeros_like(left)], axis=2)
        return lax.dynamic_update_slice_in_dim(wide, right, depth + live_cols, 2)

    def valid(width, depth):
        index = jnp.arange(width)[None, None, :, None]
        keep = index < live_cols + 2 * depth
        keep = keep & (~first_tile | (index >= depth))
        return keep & (~last_tile | (index < depth + live_cols))

    def run(ghost):
        left = lax.dynamic_slice_in_dim(from_left, left_count - ghost, ghost, 2)
        right = from_right[:, :, 0:ghost]
        current = assemble(strip, left, right, ghost)
        residual = current
        depth = ghost
        for stage in range(segments):
            out_depth = depth - 1
            conv_out = convolve(activate(current, gain), kernel)
            width = conv_out.shape[2]
            keep = valid(width, out_depth)
            if stage % 2 == 0:
                produced = jnp.where(keep, conv_out, 0.0).astype(jnp.bfloat16)
            else:
                base = residual[:, :, 1 : 1 + width]
                produced = jnp.where(keep, (base.astype(jnp.float32) + conv_out).astype(jnp.bfloat16), zero)
            if stage == segments - 1:
                return produced
            if stage % 2 == 0:
                message = jnp.stack([produced, current[:, :, 1 : 1 + width]])
            else:
                message = produced
            if out_depth == 0:
                first = produced[:, :, 0:ghost]
                last = lax.dynamic_slice_in_dim(produced, live_cols - ghost, ghost, 2)
                src, dst = stage * tiles, (stage + 1) * tiles
                new_left = hop(last, [(src + t - 1, dst + t) for t in range(1, tiles)], both)
                new_right = hop(first, [(src + t + 1, dst + t) for t in range(tiles - 1)], both)
            arrived = hop(message, [(stage, stage + 1)], "section")
            if stage % 2 == 0:
                current, residual = arrived[0], arrived[1]
            else:
                current = arrived
            if out_depth == 0:
                current = assemble(current, new_left, new_right, ghost)
                if stage % 2 == 0:
                    residual = assemble(residual, new_left, new_right, ghost)
                depth = ghost
            else:
                depth = out_depth
            residual = current if stage % 2 == 1 else residual
        return produced

    final = lax.cond(jnp.min(col_counts) >= GHOST, lambda: run(GHOST), lambda: run(1))
    spread = lax.all_to_all(final, "section", 0, 0, tiled=True)
    return spread[segments - 1 : segments]


def solution(mesh):
    return jax.shard_map(
        local,
        mesh=mesh,
        in_specs=(
            P(None, None, "tile", None),
            P(),
            P("section", None, None, None, None),
            P("section", None),
        ),
        out_specs=P("section", None, "tile", None),
        check_vma=False,
    )
```

```python
import jax
import jax.numpy as jnp
from jax import lax
from jax.sharding import PartitionSpec as P


def hop(block, pairs, axes):
    return lax.ppermute(block, axes, pairs)


def activate(values, gain):
    widened = values.astype(jnp.float32)
    scaled = widened * lax.rsqrt(jnp.mean(widened * widened, axis=-1, keepdims=True) + 1e-06) * gain
    return jax.nn.silu(scaled).astype(jnp.bfloat16)


def convolve(activated, kernel):
    frames, rows, cols_ext, channels = activated.shape
    cols = cols_ext - 2
    padded = jnp.pad(activated, ((2, 0), (1, 1), (0, 0), (0, 0)))
    shifted = jnp.concatenate([padded[:, :, k : k + cols] for k in range(3)], axis=-1)
    shifted = lax.optimization_barrier(shifted)
    stacked = jnp.concatenate([shifted[:, j : j + rows] for j in range(3)], axis=-1)
    stacked = lax.optimization_barrier(stacked)
    joined = jnp.concatenate([stacked[i : i + frames] for i in range(3)], axis=-1)
    joined = joined.reshape(frames * rows * cols, 27 * channels)
    flat = kernel.reshape(27 * channels, kernel.shape[-1])
    out = jnp.dot(joined, flat, preferred_element_type=jnp.float32)
    return out.reshape(frames, rows, cols, kernel.shape[-1])


def local(latents, col_counts, conv_weight, norm_gain):
    segments = lax.axis_size("section")
    tiles = lax.axis_size("tile")
    segment_index = lax.axis_index("section")
    tile_index = lax.axis_index("tile")
    frames_all, row_count, col_count, channels = latents.shape
    live_cols = col_counts[tile_index]
    kernel = conv_weight[0]
    gain = norm_gain[0].astype(jnp.float32)
    col_live = jnp.arange(col_count)[None, None, :, None] < live_cols
    ext_index = jnp.arange(col_count + 2)[None, None, :, None]
    zero = jnp.zeros((), jnp.bfloat16)
    both = ("section", "tile")

    def edges(block):
        first = block[:, :, 0:1]
        last = lax.dynamic_slice_in_dim(block, live_cols - 1, 1, 2)
        return first, last

    def extend(block, left, right):
        wide = jnp.concatenate([left, block, jnp.zeros_like(left)], axis=2)
        return jnp.where(ext_index == live_cols + 1, right, wide)

    def diagonal(first, last, stage):
        src, dst = stage * tiles, (stage + 1) * tiles
        left = hop(last, [(src + t - 1, dst + t) for t in range(1, tiles)], both)
        right = hop(first, [(src + t + 1, dst + t) for t in range(tiles - 1)], both)
        return left, right

    from_left = hop(latents, [(t - 1, t) for t in range(1, tiles)], "tile")
    from_right = hop(latents[:, :, 0:1], [(t + 1, t) for t in range(tiles - 1)], "tile")
    left_count = col_counts[jnp.maximum(tile_index - 1, 0)]
    left = lax.dynamic_slice_in_dim(from_left, left_count - 1, 1, 2)
    right = from_right
    stream = jnp.where(col_live, latents, zero)
    current = stream
    residual = stream
    for stage in range(segments):
        activated = activate(extend(current, left, right), gain)
        conv_out = convolve(activated, kernel)
        if stage % 2 == 0:
            produced = jnp.where(col_live, conv_out, 0.0).astype(jnp.bfloat16)
        else:
            produced = jnp.where(
                col_live, (residual.astype(jnp.float32) + conv_out).astype(jnp.bfloat16), zero
            )
        if stage == segments - 1:
            break
        first, last = edges(produced)
        left, right = diagonal(first, last, stage)
        nxt = hop(produced, [(stage, stage + 1)], "section")
        if stage % 2 == 1 and stage + 2 < segments:
            residual = hop(produced, [(stage, stage + 2)], "section")
        current = nxt
    final = produced
    spread = lax.all_to_all(final, "section", 0, 0, tiled=True)
    return spread[segments - 1 : segments]

def solution(mesh):
    return jax.shard_map(
        local,
        mesh=mesh,
        in_specs=(
            P(None, None, "tile", None),
            P(),
            P("section", None, None, None, None),
            P("section", None),
        ),
        out_specs=P("section", None, "tile", None),
        check_vma=False,
    )
```

```python
import jax
import jax.numpy as jnp
from jax import lax
from jax.sharding import PartitionSpec as P


def hop(block, pairs, axes):
    return lax.ppermute(block, axes, pairs)


def activate(values, gain):
    widened = values.astype(jnp.float32)
    scaled = widened * lax.rsqrt(jnp.mean(widened * widened, axis=-1, keepdims=True) + 1e-06) * gain
    return jax.nn.silu(scaled).astype(jnp.bfloat16)


def convolve(activated, kernel):
    frames, rows, cols_ext, channels = activated.shape
    cols = cols_ext - 2
    padded = jnp.pad(activated, ((2, 0), (1, 1), (0, 0), (0, 0)))
    shifted = jnp.concatenate([padded[:, :, k : k + cols] for k in range(3)], axis=-1)
    shifted = lax.optimization_barrier(shifted)
    taps = [
        shifted[frame_tap : frame_tap + frames, row_tap : row_tap + rows]
        for frame_tap in range(3)
        for row_tap in range(3)
    ]
    joined = jnp.concatenate(taps, axis=-1).reshape(frames * rows * cols, 27 * channels)
    flat = kernel.reshape(27 * channels, kernel.shape[-1])
    out = jnp.dot(joined, flat, preferred_element_type=jnp.float32)
    return out.reshape(frames, rows, cols, kernel.shape[-1])


def edge_terms(left, right, kernel):
    gap = jnp.zeros_like(left)
    out = convolve(jnp.concatenate([left, gap, gap, right], axis=2), kernel)
    return out[:, :, 0:1], out[:, :, 1:2]


def local(latents, col_counts, conv_weight, norm_gain):
    segments = lax.axis_size("section")
    tiles = lax.axis_size("tile")
    segment_index = lax.axis_index("section")
    tile_index = lax.axis_index("tile")
    frames_all, row_count, col_count, channels = latents.shape
    live_cols = col_counts[tile_index]
    kernel = conv_weight[0]
    gain = norm_gain[0].astype(jnp.float32)
    col_live = jnp.arange(col_count)[None, None, :, None] < live_cols
    ext_index = jnp.arange(col_count + 2)[None, None, :, None]
    zero = jnp.zeros((), jnp.bfloat16)
    both = ("section", "tile")

    def edges(block):
        first = block[:, :, 0:1]
        last = lax.dynamic_slice_in_dim(block, live_cols - 1, 1, 2)
        return first, last

    def extend(block, left, right):
        wide = jnp.concatenate([left, block, jnp.zeros_like(left)], axis=2)
        return jnp.where(ext_index == live_cols + 1, right, wide)

    def diagonal(first, last, stage):
        src, dst = stage * tiles, (stage + 1) * tiles
        left = hop(last, [(src + t - 1, dst + t) for t in range(1, tiles)], both)
        right = hop(first, [(src + t + 1, dst + t) for t in range(tiles - 1)], both)
        return left, right

    from_left = hop(latents, [(t - 1, t) for t in range(1, tiles)], "tile")
    from_right = hop(latents[:, :, 0:1], [(t + 1, t) for t in range(tiles - 1)], "tile")
    left_count = col_counts[jnp.maximum(tile_index - 1, 0)]
    left = lax.dynamic_slice_in_dim(from_left, left_count - 1, 1, 2)
    right = from_right
    stream = jnp.where(col_live, latents, zero)
    current = stream
    residual = stream
    for stage in range(segments):
        if stage == 0:
            activated = jnp.pad(activate(current, gain), ((0, 0), (0, 0), (1, 1), (0, 0)))
            conv_out = convolve(activated, kernel)
            conv_out, left, right = lax.optimization_barrier((conv_out, left, right))
            term_left, term_right = edge_terms(activate(left, gain), activate(right, gain), kernel)
            slot_index = jnp.arange(col_count)[None, None, :, None]
            conv_out = (
                conv_out
                + jnp.where(slot_index == 0, term_left, 0.0)
                + jnp.where(slot_index == live_cols - 1, term_right, 0.0)
            )
        else:
            activated = activate(extend(current, left, right), gain)
            conv_out = convolve(activated, kernel)
        if stage % 2 == 0:
            produced = jnp.where(col_live, conv_out, 0.0).astype(jnp.bfloat16)
        else:
            produced = jnp.where(
                col_live, (residual.astype(jnp.float32) + conv_out).astype(jnp.bfloat16), zero
            )
        if stage == segments - 1:
            break
        first, last = edges(produced)
        left, right = diagonal(first, last, stage)
        nxt = hop(produced, [(stage, stage + 1)], "section")
        if stage % 2 == 1 and stage + 2 < segments:
            residual = hop(produced, [(stage, stage + 2)], "section")
        current = nxt
    final = produced
    spread = lax.all_to_all(final, "section", 0, 0, tiled=True)
    return spread[segments - 1 : segments]

def solution(mesh):
    return jax.shard_map(
        local,
        mesh=mesh,
        in_specs=(
            P(None, None, "tile", None),
            P(),
            P("section", None, None, None, None),
            P("section", None),
        ),
        out_specs=P("section", None, "tile", None),
        check_vma=False,
    )
```

```python
import jax
import jax.numpy as jnp
from jax import lax
from jax.sharding import PartitionSpec as P


def hop(block, pairs, axes):
    return lax.ppermute(block, axes, pairs)


def activate(values, gain):
    widened = values.astype(jnp.float32)
    scaled = widened * lax.rsqrt(jnp.mean(widened * widened, axis=-1, keepdims=True) + 1e-06) * gain
    return jax.nn.silu(scaled).astype(jnp.bfloat16)


def norm_factor(values):
    widened = values.astype(jnp.float32)
    return lax.rsqrt(jnp.mean(widened * widened, axis=-1, keepdims=True) + 1e-06)


def apply_norm(values, factor, gain):
    return jax.nn.silu(values.astype(jnp.float32) * factor * gain).astype(jnp.bfloat16)


def convolve(raw, factor, gain, kernel):
    frames, rows, cols_ext, channels = raw.shape
    cols = cols_ext - 2
    raw = jnp.pad(raw, ((2, 0), (1, 1), (0, 0), (0, 0)))
    factor = jnp.pad(factor, ((2, 0), (1, 1), (0, 0), (0, 0)))
    shifted = jnp.concatenate(
        [apply_norm(raw[:, :, k : k + cols], factor[:, :, k : k + cols], gain) for k in range(3)], axis=-1
    )
    shifted = lax.optimization_barrier(shifted)
    taps = [
        shifted[frame_tap : frame_tap + frames, row_tap : row_tap + rows]
        for frame_tap in range(3)
        for row_tap in range(3)
    ]
    joined = jnp.concatenate(taps, axis=-1).reshape(frames * rows * cols, 27 * channels)
    flat = kernel.reshape(27 * channels, kernel.shape[-1])
    out = jnp.dot(joined, flat, preferred_element_type=jnp.float32)
    return out.reshape(frames, rows, cols, kernel.shape[-1])


def local(latents, col_counts, conv_weight, norm_gain):
    segments = lax.axis_size("section")
    tiles = lax.axis_size("tile")
    segment_index = lax.axis_index("section")
    tile_index = lax.axis_index("tile")
    frames_all, row_count, col_count, channels = latents.shape
    live_cols = col_counts[tile_index]
    kernel = conv_weight[0]
    gain = norm_gain[0].astype(jnp.float32)
    col_live = jnp.arange(col_count)[None, None, :, None] < live_cols
    ext_index = jnp.arange(col_count + 2)[None, None, :, None]
    zero = jnp.zeros((), jnp.bfloat16)
    both = ("section", "tile")

    def edges(block):
        first = block[:, :, 0:1]
        last = lax.dynamic_slice_in_dim(block, live_cols - 1, 1, 2)
        return first, last

    def extend(block, left, right):
        wide = jnp.concatenate([left, block, jnp.zeros_like(left)], axis=2)
        return jnp.where(ext_index == live_cols + 1, right, wide)

    def diagonal(first, last, stage):
        src, dst = stage * tiles, (stage + 1) * tiles
        left = hop(last, [(src + t - 1, dst + t) for t in range(1, tiles)], both)
        right = hop(first, [(src + t + 1, dst + t) for t in range(tiles - 1)], both)
        return left, right

    from_left = hop(latents, [(t - 1, t) for t in range(1, tiles)], "tile")
    from_right = hop(latents[:, :, 0:1], [(t + 1, t) for t in range(tiles - 1)], "tile")
    left_count = col_counts[jnp.maximum(tile_index - 1, 0)]
    left = lax.dynamic_slice_in_dim(from_left, left_count - 1, 1, 2)
    right = from_right
    stream = jnp.where(col_live, latents, zero)
    current = stream
    residual = stream
    for stage in range(segments):
        wide = extend(current, left, right)
        conv_out = convolve(wide, norm_factor(wide), gain, kernel)
        if stage % 2 == 0:
            produced = jnp.where(col_live, conv_out, 0.0).astype(jnp.bfloat16)
        else:
            produced = jnp.where(
                col_live, (residual.astype(jnp.float32) + conv_out).astype(jnp.bfloat16), zero
            )
        if stage == segments - 1:
            break
        first, last = edges(produced)
        left, right = diagonal(first, last, stage)
        nxt = hop(produced, [(stage, stage + 1)], "section")
        if stage % 2 == 1 and stage + 2 < segments:
            residual = hop(produced, [(stage, stage + 2)], "section")
        current = nxt
    final = produced
    spread = lax.all_to_all(final, "section", 0, 0, tiled=True)
    return spread[segments - 1 : segments]

def solution(mesh):
    return jax.shard_map(
        local,
        mesh=mesh,
        in_specs=(
            P(None, None, "tile", None),
            P(),
            P("section", None, None, None, None),
            P("section", None),
        ),
        out_specs=P("section", None, "tile", None),
        check_vma=False,
    )
```

```python
import jax
import jax.numpy as jnp
from jax import lax
from jax.sharding import PartitionSpec as P
from jax.experimental import pallas as pl
from jax.experimental.pallas import tpu as pltpu


def _touch_body(w_ref, o_ref):
    o_ref[...] = w_ref[0:8, 0:128].astype(jnp.float32)


def touch(flat):
    return pl.pallas_call(
        _touch_body,
        out_shape=jax.ShapeDtypeStruct((8, 128), jnp.float32),
        in_specs=[pl.BlockSpec(memory_space=pltpu.VMEM)],
        out_specs=pl.BlockSpec(memory_space=pltpu.VMEM),
        compiler_params=pltpu.CompilerParams(vmem_limit_bytes=48 * 1024 * 1024),
    )(flat)


def hop(block, pairs, axes):
    return lax.ppermute(block, axes, pairs)


def activate(values, gain):
    widened = values.astype(jnp.float32)
    scaled = widened * lax.rsqrt(jnp.mean(widened * widened, axis=-1, keepdims=True) + 1e-06) * gain
    return jax.nn.silu(scaled).astype(jnp.bfloat16)


def convolve(activated, kernel):
    frames, rows, cols_ext, channels = activated.shape
    cols = cols_ext - 2
    padded = jnp.pad(activated, ((2, 0), (1, 1), (0, 0), (0, 0)))
    shifted = jnp.concatenate([padded[:, :, k : k + cols] for k in range(3)], axis=-1)
    shifted = lax.optimization_barrier(shifted)
    taps = [
        shifted[frame_tap : frame_tap + frames, row_tap : row_tap + rows]
        for frame_tap in range(3)
        for row_tap in range(3)
    ]
    joined = jnp.concatenate(taps, axis=-1).reshape(frames * rows * cols, 27 * channels)
    flat = kernel.reshape(27 * channels, kernel.shape[-1])
    out = jnp.dot(joined, flat, preferred_element_type=jnp.float32)
    return out.reshape(frames, rows, cols, kernel.shape[-1])


def local(latents, col_counts, conv_weight, norm_gain):
    segments = lax.axis_size("section")
    tiles = lax.axis_size("tile")
    segment_index = lax.axis_index("section")
    tile_index = lax.axis_index("tile")
    frames_all, row_count, col_count, channels = latents.shape
    live_cols = col_counts[tile_index]
    kernel = conv_weight[0]
    gain = norm_gain[0].astype(jnp.float32)
    col_live = jnp.arange(col_count)[None, None, :, None] < live_cols
    ext_index = jnp.arange(col_count + 2)[None, None, :, None]
    zero = jnp.zeros((), jnp.bfloat16)
    both = ("section", "tile")

    def edges(block):
        first = block[:, :, 0:1]
        last = lax.dynamic_slice_in_dim(block, live_cols - 1, 1, 2)
        return first, last

    def extend(block, left, right):
        wide = jnp.concatenate([left, block, jnp.zeros_like(left)], axis=2)
        return jnp.where(ext_index == live_cols + 1, right, wide)

    def diagonal(first, last, stage):
        src, dst = stage * tiles, (stage + 1) * tiles
        left = hop(last, [(src + t - 1, dst + t) for t in range(1, tiles)], both)
        right = hop(first, [(src + t + 1, dst + t) for t in range(tiles - 1)], both)
        return left, right

    from_left = hop(latents, [(t - 1, t) for t in range(1, tiles)], "tile")
    from_right = hop(latents[:, :, 0:1], [(t + 1, t) for t in range(tiles - 1)], "tile")
    left_count = col_counts[jnp.maximum(tile_index - 1, 0)]
    left = lax.dynamic_slice_in_dim(from_left, left_count - 1, 1, 2)
    right = from_right
    stream = jnp.where(col_live, latents, zero)
    touched = touch(kernel.reshape(-1, kernel.shape[-1]))
    stream, touched = lax.optimization_barrier((stream, touched))
    current = stream
    residual = stream
    for stage in range(segments):
        activated = activate(extend(current, left, right), gain)
        conv_out = convolve(activated, kernel)
        if stage % 2 == 0:
            produced = jnp.where(col_live, conv_out, 0.0).astype(jnp.bfloat16)
        else:
            produced = jnp.where(
                col_live, (residual.astype(jnp.float32) + conv_out).astype(jnp.bfloat16), zero
            )
        if stage == segments - 1:
            break
        first, last = edges(produced)
        left, right = diagonal(first, last, stage)
        nxt = hop(produced, [(stage, stage + 1)], "section")
        if stage % 2 == 1 and stage + 2 < segments:
            residual = hop(produced, [(stage, stage + 2)], "section")
        current = nxt
    final = produced
    spread = lax.all_to_all(final, "section", 0, 0, tiled=True)
    return spread[segments - 1 : segments] + (touched[0, 0] * 0.0).astype(jnp.bfloat16)

def solution(mesh):
    return jax.shard_map(
        local,
        mesh=mesh,
        in_specs=(
            P(None, None, "tile", None),
            P(),
            P("section", None, None, None, None),
            P("section", None),
        ),
        out_specs=P("section", None, "tile", None),
        check_vma=False,
    )
```

```python
import jax
import jax.numpy as jnp
from jax import lax
from jax.sharding import PartitionSpec as P


def hop(block, pairs, axes):
    return lax.ppermute(block, axes, pairs)


def activate(values, gain):
    widened = values.astype(jnp.float32)
    scaled = widened * lax.rsqrt(jnp.mean(widened * widened, axis=-1, keepdims=True) + 1e-06) * gain
    return jax.nn.silu(scaled).astype(jnp.bfloat16)


def convolve(activated, kernel):
    frames, rows, cols_ext, channels = activated.shape
    cols = cols_ext - 2
    padded = jnp.pad(activated, ((2, 0), (1, 1), (0, 0), (0, 0)))
    shifted = jnp.concatenate([padded[:, :, k : k + cols] for k in range(3)], axis=-1)
    shifted = lax.optimization_barrier(shifted)
    taps = [
        shifted[frame_tap : frame_tap + frames, row_tap : row_tap + rows]
        for frame_tap in range(3)
        for row_tap in range(3)
    ]
    joined = jnp.concatenate(taps, axis=-1).reshape(frames * rows * cols, 27 * channels)
    flat = kernel.reshape(27 * channels, kernel.shape[-1])
    out = jnp.dot(joined, flat, preferred_element_type=jnp.float32)
    return out.reshape(frames, rows, cols, kernel.shape[-1])


def local(latents, col_counts, conv_weight, norm_gain):
    segments = lax.axis_size("section")
    tiles = lax.axis_size("tile")
    segment_index = lax.axis_index("section")
    tile_index = lax.axis_index("tile")
    frames_all, row_count, col_count, channels = latents.shape
    live_cols = col_counts[tile_index]
    kernel = conv_weight[0]
    gain = norm_gain[0].astype(jnp.float32)
    col_live = jnp.arange(col_count)[None, None, :, None] < live_cols
    ext_index = jnp.arange(col_count + 2)[None, None, :, None]
    zero = jnp.zeros((), jnp.bfloat16)
    both = ("section", "tile")

    def edges(block):
        first = block[:, :, 0:1]
        last = lax.dynamic_slice_in_dim(block, live_cols - 1, 1, 2)
        return first, last

    def extend(block, left, right):
        wide = jnp.concatenate([left, block, jnp.zeros_like(left)], axis=2)
        return jnp.where(ext_index == live_cols + 1, right, wide)

    def diagonal(first, last, stage):
        src, dst = stage * tiles, (stage + 1) * tiles
        left = hop(last, [(src + t - 1, dst + t) for t in range(1, tiles)], both)
        right = hop(first, [(src + t + 1, dst + t) for t in range(tiles - 1)], both)
        return left, right

    from_left = hop(latents, [(t - 1, t) for t in range(1, tiles)], "tile")
    from_right = hop(latents[:, :, 0:1], [(t + 1, t) for t in range(tiles - 1)], "tile")
    left_count = col_counts[jnp.maximum(tile_index - 1, 0)]
    left = lax.dynamic_slice_in_dim(from_left, left_count - 1, 1, 2)
    right = from_right
    stream = jnp.where(col_live, latents, zero)
    current = stream
    residual = stream
    for stage in range(segments):
        activated = activate(extend(current, left, right), gain)
        conv_out = convolve(activated, kernel)
        if stage % 2 == 0:
            produced = jnp.where(col_live, conv_out, 0.0).astype(jnp.bfloat16)
        else:
            produced = jnp.where(
                col_live, (residual.astype(jnp.float32) + conv_out).astype(jnp.bfloat16), zero
            )
        if stage == segments - 1:
            break
        first, last = edges(produced)
        left, right = diagonal(first, last, stage)
        if stage % 2 == 0:
            arrived = hop(jnp.stack([produced, residual]), [(stage, stage + 1)], "section")
            current, residual = arrived[0], arrived[1]
        else:
            current = hop(produced, [(stage, stage + 1)], "section")
            residual = current
    final = produced
    spread = lax.all_to_all(final, "section", 0, 0, tiled=True)
    return spread[segments - 1 : segments]

def solution(mesh):
    return jax.shard_map(
        local,
        mesh=mesh,
        in_specs=(
            P(None, None, "tile", None),
            P(),
            P("section", None, None, None, None),
            P("section", None),
        ),
        out_specs=P("section", None, "tile", None),
        check_vma=False,
    )
```

```python
import jax
import jax.numpy as jnp
from jax import lax
from jax.sharding import PartitionSpec as P


def hop(block, pairs, axes):
    return lax.ppermute(block, axes, pairs)


def activate(values, gain):
    widened = values.astype(jnp.float32)
    scaled = widened * lax.rsqrt(jnp.mean(widened * widened, axis=-1, keepdims=True) + 1e-06) * gain
    return jax.nn.silu(scaled).astype(jnp.bfloat16)


def convolve(activated, kernel):
    frames, rows, cols_ext, channels = activated.shape
    cols = cols_ext - 2
    padded = jnp.pad(activated, ((2, 0), (1, 1), (0, 0), (0, 0)))
    shifted = jnp.concatenate([padded[:, :, k : k + cols] for k in range(3)], axis=-1)
    shifted = lax.optimization_barrier(shifted)
    taps = [
        shifted[frame_tap : frame_tap + frames, row_tap : row_tap + rows]
        for frame_tap in range(3)
        for row_tap in range(3)
    ]
    joined = jnp.concatenate(taps, axis=-1).reshape(frames * rows * cols, 27 * channels)
    flat = kernel.reshape(27 * channels, kernel.shape[-1])
    out = jnp.dot(joined, flat, preferred_element_type=jnp.float32)
    return out.reshape(frames, rows, cols, kernel.shape[-1])


def local(latents, col_counts, conv_weight, norm_gain):
    segments = lax.axis_size("section")
    tiles = lax.axis_size("tile")
    segment_index = lax.axis_index("section")
    tile_index = lax.axis_index("tile")
    frames_all, row_count, col_count, channels = latents.shape
    live_cols = col_counts[tile_index]
    kernel = conv_weight[0]
    gain = norm_gain[0].astype(jnp.float32)
    col_live = jnp.arange(col_count)[None, None, :, None] < live_cols
    ext_index = jnp.arange(col_count + 2)[None, None, :, None]
    zero = jnp.zeros((), jnp.bfloat16)
    both = ("section", "tile")

    def edges(block):
        first = block[:, :, 0:1]
        last = lax.dynamic_slice_in_dim(block, live_cols - 1, 1, 2)
        return first, last

    def extend(block, left, right):
        wide = jnp.concatenate([left, block, jnp.zeros_like(left)], axis=2)
        return jnp.where(ext_index == live_cols + 1, right, wide)

    def diagonal(first, last, stage):
        src, dst = stage * tiles, (stage + 1) * tiles
        left = hop(last, [(src + t - 1, dst + t) for t in range(1, tiles)], both)
        right = hop(first, [(src + t + 1, dst + t) for t in range(tiles - 1)], both)
        return left, right

    left_count = col_counts[jnp.maximum(tile_index - 1, 0)]
    masked = jnp.where(col_live, latents, zero)
    latents, masked, gain, live_cols, left_count, col_live = lax.optimization_barrier(
        (latents, masked, gain, live_cols, left_count, col_live)
    )
    from_left = hop(latents, [(t - 1, t) for t in range(1, tiles)], "tile")
    from_right = hop(latents[:, :, 0:1], [(t + 1, t) for t in range(tiles - 1)], "tile")
    left = lax.dynamic_slice_in_dim(from_left, left_count - 1, 1, 2)
    right = from_right
    stream = masked
    current = stream
    residual = stream
    for stage in range(segments):
        activated = activate(extend(current, left, right), gain)
        conv_out = convolve(activated, kernel)
        if stage % 2 == 0:
            produced = jnp.where(col_live, conv_out, 0.0).astype(jnp.bfloat16)
        else:
            produced = jnp.where(
                col_live, (residual.astype(jnp.float32) + conv_out).astype(jnp.bfloat16), zero
            )
        if stage == segments - 1:
            break
        first, last = edges(produced)
        left, right = diagonal(first, last, stage)
        nxt = hop(produced, [(stage, stage + 1)], "section")
        if stage % 2 == 1 and stage + 2 < segments:
            residual = hop(produced, [(stage, stage + 2)], "section")
        current = nxt
    final = produced
    spread = lax.all_to_all(final, "section", 0, 0, tiled=True)
    return spread[segments - 1 : segments]

def solution(mesh):
    return jax.shard_map(
        local,
        mesh=mesh,
        in_specs=(
            P(None, None, "tile", None),
            P(),
            P("section", None, None, None, None),
            P("section", None),
        ),
        out_specs=P("section", None, "tile", None),
        check_vma=False,
    )
```
